128 devices in a mesh: section: 4 (over x), expert: 32 (over z, y, core).
Axes of the slice: x: 4, y: 4, z: 4, core: 2. Of those that a mesh axis runs over, the one named last changes fastest.
Arguments:
- hidden_in: bfloat16 [4, 4096, 2880], P('section', 'expert')
- norm_gain: float32 [4, 2880], P('section'), may hold values from 0.25 to 1.75
- out_grad: bfloat16 [4, 4096, 2880], P('section', 'expert'), may hold values from -6 to 6
- expert_ids: int32 [4, 4096, 4], P('section', 'expert'), may hold values from 0 to 31, all different within a row; in each aligned block of 128 rows (0 to 127, 128 to 255, ..., all dimensions but the last counted through in order) at most 20 rows name the same one
- route_weights: float32 [4, 4096, 4], P('section', 'expert'), may hold values from 0 to 1, as said below
- w_gate_up: bfloat16 [4, 32, 2880, 2880], P('section', 'expert'), may hold values from -0.109375 to 0.109375
- w_down: bfloat16 [4, 32, 1440, 2880], P('section', 'expert'), may hold values from -0.15625 to 0.15625
Outputs:
- input_grad: bfloat16 [4, 4096, 2880], P('section', 'expert')
The draws below stay inside these ranges and needn't reach their ends.
Inputs may be any that keep to these rules, and one draw needn't show every extreme that they name: `expert_ids`: each token names 4 different experts. The 128 tokens of one index of expert in one section name any one expert at most 20 times, a bound that some block reaches. `route_weights`: each token's 4 weights are positive and sum to one.
All inputs are finite; a program needn't handle non-finite values.
Results may differ from the reference program's by a relative error of at most 0.0047.
Values may be sent and summed in bfloat16 or wider, within the bound.
No kernel may reach another device: no remote copies, remote signals or barrier semaphores. Data moves between devices by JAX's collectives and lax.ppermute only.
A program may use at most 128 MiB of HBM per device.

```python
import math
import jax
import jax.numpy as jnp
import numpy as np
from jax import lax

D = 2880
FFW = 1440
TOPK = 4
TOK_DEV = 128
SECTIONS = 4
EXPERTS = 32
TOKENS = 4096
CAP = 20


def draw_hidden_in(key, part):
    keys = jax.random.split(key, 3)
    row_scale = jnp.exp(jax.random.uniform(keys[1], (SECTIONS, TOKENS, 1), jnp.float32, jnp.log(0.5), jnp.log(5.0)))
    col_scale = jnp.exp(jax.random.uniform(keys[2], (1, 1, D), jnp.float32, jnp.log(0.3), jnp.log(3.0)))
    base = jax.random.normal(keys[0], (SECTIONS, TOKENS, D), jnp.float32)
    return (base * row_scale * col_scale).astype(jnp.bfloat16)


def draw_route_weights(key, part):
    logits = jax.random.normal(key, (SECTIONS, TOKENS, TOPK), jnp.float32)
    return jax.nn.softmax(logits, axis=-1)


def level_of(key, dims, cuts, least, largest):
    factor_of, own = 1.0, jax.random.fold_in(key, 6)
    for dim, blocks in cuts:
        heights = jnp.exp(jax.random.uniform(jax.random.fold_in(own, dim), (blocks,), jnp.float32, least / len(cuts), largest / len(cuts)))
        factor_of = factor_of * jnp.repeat(heights, dims[dim] // blocks).reshape([-1 if axis == dim else 1 for axis in range(len(dims))])
    return factor_of


def routed_block(key, own, number, rows, amount, top, reach, lean):
    sequence = jax.random.permutation(key, amount)
    crowded, ordinary = portions_of(amount, rows * top, reach, lean, True), portions_of(amount, rows * top, reach, lean, False)
    places = jnp.arange(amount)

    def named(sizes, turn):
        used = int((sizes > 0).sum())
        fixed = max(1, used // 4)
        shifted = fixed + (places - fixed + turn * (used - fixed)) % max(1, amount - fixed)
        return jnp.zeros((amount,), jnp.int32).at[sequence[jnp.where(places < fixed, places, shifted)]].set(jnp.asarray(sizes, jnp.int32))

    sizes = jnp.where(number % 4 == 0, named(crowded, number // 4), named(ordinary, number - number // 4 - 1))
    mixed = jax.random.permutation(jax.random.fold_in(own, 3), amount)
    giver, taker = mixed[0:amount // 2 * 2:2], mixed[1:amount // 2 * 2:2]
    margin = jnp.minimum(sizes[giver] - 1, reach - sizes[taker]) // 2
    margin = jnp.where((giver == sequence[0]) | (taker == sequence[0]) | (sizes[taker] == 0), 0, jnp.maximum(margin, 0))
    shifted = jax.random.randint(jax.random.fold_in(own, 4), (amount // 2,), 0, 1 << 20) % (margin + 1)
    sizes = sizes.at[giver].add(-shifted).at[taker].add(shifted)
    items = jnp.searchsorted(jnp.cumsum(sizes), jnp.arange(rows * top), side="right").astype(jnp.int32)
    table = items.reshape(top, rows).T
    table = table[jax.random.permutation(jax.random.fold_in(own, 1), rows)]
    turn = jax.random.randint(jax.random.fold_in(own, 2), (rows, 1), 0, top)
    return jnp.take_along_axis(table, (jnp.arange(top)[None, :] + turn) % top, axis=1)


def portions_of(number_of, total, most, lean, full):
    weights = [(1 << 20) // math.isqrt(rank ** lean) + 1 for rank in range(1, number_of + 1)]
    largest = most if full else min(most, max(-(-total // number_of), total * weights[0] // sum(weights)))
    least = 1 if total - largest >= number_of - 1 else 0
    holding, rest = [largest] + [least] * (number_of - 1), total - largest - least * (number_of - 1)
    while rest > 0:
        free = [i for i in range(1, number_of) if holding[i] < largest] or [i for i in range(1, number_of) if holding[i] < most]
        mass, left = sum([weights[i] for i in free]), rest
        for i in free:
            addition = min(most - holding[i], max(1, left * weights[i] // mass), rest)
            holding[i] = holding[i] + addition
            rest = rest - addition
    return np.array(holding)


def scatter_about(rng, shape, spread, most, pieces=(), kind=jnp.bfloat16):
    drawn = jax.random.normal(rng, shape, jnp.float32) * spread
    if len(pieces) > 0:
        drawn = level_of(rng, shape, pieces, -0.22, 0.18) * drawn
    return jnp.clip(drawn, min=-most, max=most).astype(kind)


def setup_inputs(seed: int = 0) -> dict:
    arg_keys = jax.random.split(jax.random.key(seed), 8)
    hidden_in = draw_hidden_in(jax.random.fold_in(arg_keys[7], 71), 0)
    norm_gain = jnp.clip(1.0 + 0.15 * jax.random.normal(arg_keys[1], (SECTIONS, D), jnp.float32), 0.25, 1.75)
    out_grad = scatter_about(arg_keys[2], (SECTIONS, TOKENS, D), 1.0, 6.0, ((0, 4), (1, 32)))
    expert_ids_keys = jax.random.split(jax.random.fold_in(arg_keys[3], 1), SECTIONS * TOKENS // TOK_DEV)
    expert_ids_turns = jax.random.permutation(jax.random.fold_in(arg_keys[3], 3), SECTIONS * TOKENS // TOK_DEV)
    expert_ids = jax.vmap(lambda own, number: routed_block(jax.random.fold_in(arg_keys[3], 2), own, number, TOK_DEV, EXPERTS, TOPK, CAP, 2))(expert_ids_keys, expert_ids_turns).reshape((SECTIONS, TOKENS, TOPK))
    route_weights = draw_route_weights(jax.random.fold_in(arg_keys[7], 71), 0)
    w_gate_up = scatter_about(arg_keys[5], (SECTIONS, EXPERTS, D, 2 * FFW), D ** -0.5, 0.109375, ((0, 4), (1, 32)))
    w_down = scatter_about(arg_keys[6], (SECTIONS, EXPERTS, FFW, D), FFW ** -0.5, 0.15625, ((0, 4), (1, 32)))
    return dict(hidden_in=hidden_in, norm_gain=norm_gain, out_grad=out_grad, expert_ids=expert_ids, route_weights=route_weights, w_gate_up=w_gate_up, w_down=w_down)


glu_alpha = 1.702
norm_eps = 1e-05

def expert_backward(packed):
    rows_in, grad_rows, gate_up, down_proj = packed
    preact = jnp.dot(rows_in, gate_up, preferred_element_type=jnp.float32)
    dact = jnp.dot(grad_rows, down_proj.T, preferred_element_type=jnp.float32)
    half = down_proj.shape[0]
    gate = preact[:, :half]
    up_part = preact[:, half:]
    sig = jax.nn.sigmoid(glu_alpha * gate)
    dgate = dact * (up_part + 1.0) * (sig + glu_alpha * gate * sig * (1.0 - sig))
    dup = dact * gate * sig
    dpre = jnp.concatenate([dgate, dup], axis=1).astype(jnp.bfloat16)
    return jnp.dot(dpre, gate_up.T, preferred_element_type=jnp.float32).astype(jnp.bfloat16)

def section_pass(tokens, gain_vector_row, incoming_gradient, routes, weights, gate_up, down_proj):
    input_single_precision = tokens.astype(jnp.float32)
    inverse_root_mean = lax.rsqrt(lax.optimization_barrier(jnp.mean(input_single_precision * input_single_precision, axis=-1, keepdims=True)) + norm_eps)
    normalized_input = input_single_precision * inverse_root_mean
    rescaled_input = (normalized_input * gain_vector_row[None, :]).astype(jnp.bfloat16)
    tok_count = tokens.shape[0]
    flat_ids = routes.reshape(-1).astype(jnp.int32)
    assign = flat_ids.shape[0]
    one_hot = (flat_ids[:, None] == jnp.arange(EXPERTS, dtype=jnp.int32)[None, :]).astype(jnp.int32)
    slot_rank = lax.optimization_barrier(jnp.sum((jnp.cumsum(one_hot, axis=0) - one_hot) * one_hot, axis=1)).astype(jnp.int32)
    per_expert = EXPERTS * CAP
    slot_index = (flat_ids * per_expert + slot_rank).astype(jnp.int32)
    source_of = jnp.full((EXPERTS * per_expert,), assign, jnp.int32).at[slot_index].set(jnp.arange(assign, dtype=jnp.int32))
    token_of = (source_of // TOPK).astype(jnp.int32)
    normed_pad = jnp.concatenate([rescaled_input, jnp.zeros((1, D), jnp.bfloat16)], axis=0)
    grad_pad = jnp.concatenate([incoming_gradient.astype(jnp.float32), jnp.zeros((1, D), jnp.float32)], axis=0)
    weight_pad = jnp.concatenate([weights.reshape(-1).astype(jnp.float32), jnp.zeros((1,), jnp.float32)])
    rows_in = normed_pad[token_of].reshape(EXPERTS, per_expert, D)
    grad_rows = (weight_pad[source_of][:, None] * grad_pad[token_of]).astype(jnp.bfloat16).reshape(EXPERTS, per_expert, D)
    slots = lax.map(expert_backward, (rows_in, grad_rows, gate_up, down_proj))
    gathered = slots.reshape(-1, D)[slot_index].astype(jnp.float32)
    dnorm = lax.optimization_barrier(jnp.sum(gathered.reshape(tok_count, TOPK, D), axis=1))
    normalized_input_gradient = dnorm * gain_vector_row[None, :]
    projected_rows = lax.optimization_barrier(jnp.mean(normalized_input_gradient * normalized_input, axis=-1, keepdims=True))
    return (incoming_gradient.astype(jnp.float32) + inverse_root_mean * (normalized_input_gradient - normalized_input * projected_rows)).astype(jnp.bfloat16)

def reference(hidden_in, norm_gain, out_grad, expert_ids, route_weights, w_gate_up, w_down):
    results = []
    for section_num in range(SECTIONS):
        results.append(section_pass(hidden_in[section_num], norm_gain[section_num], out_grad[section_num], expert_ids[section_num], route_weights[section_num], w_gate_up[section_num], w_down[section_num]))
    stacked = jnp.stack(results, axis=0)
    return jnp.roll(stacked, -1, axis=0)
```

```python
import jax
import jax.numpy as jnp
from jax import lax
from jax.sharding import PartitionSpec as P

glu_alpha = 1.702
norm_eps = 1e-05
ROW_TILE = 8


def shifted(value, axis, steps):
    count = lax.axis_size(axis)
    pairs = [(source, (source + steps) % count) for source in range(count)]
    return lax.ppermute(value, axis, pairs)


def expert_backward(rows_in, grad_rows, gate_up, down_proj):
    preact = jnp.dot(rows_in, gate_up, preferred_element_type=jnp.float32)
    dact = lax.dot_general(
        grad_rows, down_proj, (((1,), (1,)), ((), ())), preferred_element_type=jnp.float32
    )
    half = down_proj.shape[0]
    gate = preact[:, :half]
    up_part = preact[:, half:]
    sig = jax.nn.sigmoid(glu_alpha * gate)
    dgate = dact * (up_part + 1.0) * (sig + glu_alpha * gate * sig * (1.0 - sig))
    dup = dact * gate * sig
    dpre = jnp.concatenate([dgate, dup], axis=1).astype(jnp.bfloat16)
    result = lax.dot_general(
        dpre, gate_up, (((1,), (1,)), ((), ())), preferred_element_type=jnp.float32
    )
    return result.astype(jnp.bfloat16)


def exchange(slab):
    return lax.all_to_all(slab, "expert", split_axis=0, concat_axis=0, tiled=True)


def per_device(hidden_in, norm_gain, out_grad, expert_ids, route_weights, w_gate_up, w_down):
    tokens = hidden_in[0]
    gain_vector_row = norm_gain[0]
    incoming_gradient = out_grad[0]
    routes = expert_ids[0]
    weights = route_weights[0]
    gate_up = w_gate_up[0, 0]
    down_proj = w_down[0, 0]
    tok_count, feat_width = tokens.shape
    top_count = routes.shape[1]
    experts = lax.axis_size("expert")
    bound = max(2, tok_count * top_count * 5 // (4 * experts))
    capacity = -(-bound // ROW_TILE) * ROW_TILE

    input_single_precision = tokens.astype(jnp.float32)
    inverse_root_mean = lax.rsqrt(
        jnp.mean(input_single_precision * input_single_precision, axis=-1, keepdims=True) + norm_eps
    )
    normalized_input = input_single_precision * inverse_root_mean
    rescaled_input = (normalized_input * gain_vector_row[None, :]).astype(jnp.bfloat16)

    flat_ids = routes.reshape(-1)
    assign = flat_ids.shape[0]
    one_hot = (flat_ids[:, None] == jnp.arange(experts, dtype=jnp.int32)[None, :]).astype(jnp.int32)
    slot_rank = jnp.sum((jnp.cumsum(one_hot, axis=0) - one_hot) * one_hot, axis=1)
    slot_index = flat_ids * capacity + slot_rank
    source_of = (
        jnp.full((experts * capacity,), assign, jnp.int32)
        .at[slot_index]
        .set(jnp.arange(assign, dtype=jnp.int32))
    )
    token_of = source_of // top_count
    normed_pad = jnp.concatenate([rescaled_input, jnp.zeros((1, feat_width), jnp.bfloat16)], axis=0)
    grad_pad = jnp.concatenate([incoming_gradient, jnp.zeros((1, feat_width), jnp.bfloat16)], axis=0)
    weight_pad = jnp.concatenate([weights.reshape(-1), jnp.zeros((1,), jnp.float32)])
    inputs_slab = normed_pad[token_of].reshape(experts, capacity, feat_width)
    grads_slab = (
        (weight_pad[source_of][:, None] * grad_pad[token_of].astype(jnp.float32))
        .astype(jnp.bfloat16)
        .reshape(experts, capacity, feat_width)
    )
    arrived_inputs = exchange(inputs_slab).reshape(experts * capacity, feat_width)
    arrived_grads = exchange(grads_slab).reshape(experts * capacity, feat_width)
    computed = expert_backward(arrived_inputs, arrived_grads, gate_up, down_proj)
    returned = exchange(computed.reshape(experts, capacity, feat_width)).reshape(
        experts * capacity, feat_width
    )
    slots_by_token = slot_index.reshape(tok_count, top_count)
    dnorm = returned[slots_by_token[:, 0]].astype(jnp.float32)
    for k in range(1, top_count):
        dnorm = dnorm + returned[slots_by_token[:, k]].astype(jnp.float32)
    normalized_input_gradient = dnorm * gain_vector_row[None, :]
    projected_rows = jnp.mean(normalized_input_gradient * normalized_input, axis=-1, keepdims=True)
    section_gradient = (
        incoming_gradient.astype(jnp.float32)
        + inverse_root_mean * (normalized_input_gradient - normalized_input * projected_rows)
    ).astype(jnp.bfloat16)
    return shifted(section_gradient[None], "section", -1)


def solution(mesh):
    return jax.shard_map(
        per_device,
        mesh=mesh,
        in_specs=(
            P("section", "expert", None),
            P("section", None),
            P("section", "expert", None),
            P("section", "expert", None),
            P("section", "expert", None),
            P("section", "expert", None, None),
            P("section", "expert", None, None),
        ),
        out_specs=P("section", "expert", None),
        check_vma=False,
    )
```

```python
import jax
import jax.numpy as jnp
from jax import lax
from jax.experimental.layout import Layout, with_layout_constraint
from jax.sharding import PartitionSpec as P

glu_alpha = 1.702
norm_eps = 1e-05
ROW_TILE = 8


def shifted(value, axis, steps):
    count = lax.axis_size(axis)
    pairs = [(source, (source + steps) % count) for source in range(count)]
    return lax.ppermute(value, axis, pairs)


def expert_backward(rows_in, grad_rows, gate_up, down_proj):
    preact = jnp.dot(rows_in, gate_up, preferred_element_type=jnp.float32)
    dact = lax.dot_general(
        grad_rows, down_proj, (((1,), (1,)), ((), ())), preferred_element_type=jnp.float32
    )
    half = down_proj.shape[0]
    gate = preact[:, :half]
    up_part = preact[:, half:]
    sig = jax.nn.sigmoid(glu_alpha * gate)
    dgate = dact * (up_part + 1.0) * (sig + glu_alpha * gate * sig * (1.0 - sig))
    dup = dact * gate * sig
    dpre = jnp.concatenate([dgate, dup], axis=1).astype(jnp.bfloat16)
    result_t = lax.dot_general(
        gate_up, dpre, (((1,), (1,)), ((), ())), preferred_element_type=jnp.float32
    )
    return row_major(result_t.astype(jnp.bfloat16).T)


def row_major(value):
    return with_layout_constraint(value, Layout(tuple(range(value.ndim))))


def exchange(slab):
    return lax.all_to_all(slab, "expert", split_axis=0, concat_axis=0, tiled=True)


def per_device(hidden_in, norm_gain, out_grad, expert_ids, route_weights, w_gate_up, w_down):
    tokens = hidden_in[0]
    gain_vector_row = norm_gain[0]
    incoming_gradient = out_grad[0]
    routes = expert_ids[0]
    weights = route_weights[0]
    gate_up = w_gate_up[0, 0]
    down_proj = w_down[0, 0]
    tok_count, feat_width = tokens.shape
    top_count = routes.shape[1]
    experts = lax.axis_size("expert")
    bound = max(2, tok_count * top_count * 5 // (4 * experts))
    capacity = -(-bound // ROW_TILE) * ROW_TILE

    input_single_precision = tokens.astype(jnp.float32)
    inverse_root_mean = lax.rsqrt(
        jnp.mean(input_single_precision * input_single_precision, axis=-1, keepdims=True) + norm_eps
    )
    normalized_input = input_single_precision * inverse_root_mean
    rescaled_input = (normalized_input * gain_vector_row[None, :]).astype(jnp.bfloat16)

    flat_ids = routes.reshape(-1)
    one_hot = (flat_ids[:, None] == jnp.arange(experts, dtype=jnp.int32)[None, :]).astype(jnp.int32)
    slot_rank = jnp.sum((jnp.cumsum(one_hot, axis=0) - one_hot) * one_hot, axis=1)
    slot_index = (flat_ids * capacity + slot_rank).reshape(tok_count, top_count)
    slot_ids = jnp.arange(experts * capacity, dtype=jnp.int32)
    hits = slot_index[:, :, None] == slot_ids[None, None, :]
    placement = jnp.any(hits, axis=1)
    slot_weight = jnp.sum(jnp.where(hits, weights[:, :, None], 0.0), axis=(0, 1))
    placement_bf16 = placement.astype(jnp.bfloat16)
    pick = (((0,), (0,)), ((), ()))
    inputs_slab = lax.dot_general(
        rescaled_input, placement_bf16, pick, preferred_element_type=jnp.float32
    ).astype(jnp.bfloat16).T
    inputs_slab = row_major(inputs_slab)
    grads_slab = (
        lax.dot_general(incoming_gradient, placement_bf16, pick, preferred_element_type=jnp.float32)
        * slot_weight[None, :]
    ).astype(jnp.bfloat16).T
    grads_slab = row_major(grads_slab)
    arrived_inputs = exchange(inputs_slab.reshape(experts, capacity, feat_width))
    arrived_grads = exchange(grads_slab.reshape(experts, capacity, feat_width))
    computed = expert_backward(
        arrived_inputs.reshape(experts * capacity, feat_width),
        arrived_grads.reshape(experts * capacity, feat_width),
        gate_up,
        down_proj,
    )
    returned = exchange(computed.reshape(experts, capacity, feat_width)).reshape(
        experts * capacity, feat_width
    )
    dnorm = jnp.dot(placement_bf16, returned, preferred_element_type=jnp.float32)
    normalized_input_gradient = dnorm * gain_vector_row[None, :]
    projected_rows = jnp.mean(normalized_input_gradient * normalized_input, axis=-1, keepdims=True)
    section_gradient = (
        incoming_gradient.astype(jnp.float32)
        + inverse_root_mean * (normalized_input_gradient - normalized_input * projected_rows)
    ).astype(jnp.bfloat16)
    return shifted(section_gradient[None], "section", -1)


def solution(mesh):
    return jax.shard_map(
        per_device,
        mesh=mesh,
        in_specs=(
            P("section", "expert", None),
            P("section", None),
            P("section", "expert", None),
            P("section", "expert", None),
            P("section", "expert", None),
            P("section", "expert", None, None),
            P("section", "expert", None, None),
        ),
        out_specs=P("section", "expert", None),
        check_vma=False,
    )
```

```python
import jax
import jax.numpy as jnp
from jax import lax
from jax.experimental.layout import Layout, with_layout_constraint
from jax.sharding import PartitionSpec as P

glu_alpha = 1.702
norm_eps = 1e-05
ROW_TILE = 8
LANES = 128


def shifted(value, axis, steps):
    count = lax.axis_size(axis)
    pairs = [(source, (source + steps) % count) for source in range(count)]
    return lax.ppermute(value, axis, pairs)


def expert_backward(rows_in, grad_rows, gate_up, down_proj):
    preact = jnp.dot(rows_in, gate_up, preferred_element_type=jnp.float32)
    dact = lax.dot_general(
        grad_rows, down_proj, (((1,), (1,)), ((), ())), preferred_element_type=jnp.float32
    )
    half = down_proj.shape[0]
    gate = preact[:, :half]
    up_part = preact[:, half:]
    sig = jax.nn.sigmoid(glu_alpha * gate)
    dgate = dact * (up_part + 1.0) * (sig + glu_alpha * gate * sig * (1.0 - sig))
    dup = dact * gate * sig
    dpre = jnp.concatenate([dgate, dup], axis=1).astype(jnp.bfloat16)
    result_t = lax.dot_general(
        gate_up, dpre, (((1,), (1,)), ((), ())), preferred_element_type=jnp.float32
    )
    return row_major(result_t.astype(jnp.bfloat16).T)


def row_major(value):
    return with_layout_constraint(value, Layout(tuple(range(value.ndim))))


def exchange(rows, groups):
    width = rows.shape[1]
    per_group = rows.shape[0] // groups
    dense = rows.reshape(groups, per_group * width // LANES, LANES)
    moved = lax.all_to_all(dense, "expert", split_axis=0, concat_axis=0, tiled=True)
    return moved.reshape(groups * per_group, width)


def per_device(hidden_in, norm_gain, out_grad, expert_ids, route_weights, w_gate_up, w_down):
    tokens = hidden_in[0]
    gain_vector_row = norm_gain[0]
    incoming_gradient = out_grad[0]
    routes = expert_ids[0]
    weights = route_weights[0]
    gate_up = w_gate_up[0, 0]
    down_proj = w_down[0, 0]
    tok_count, feat_width = tokens.shape
    top_count = routes.shape[1]
    experts = lax.axis_size("expert")
    bound = max(2, tok_count * top_count * 5 // (4 * experts))
    capacity = bound

    input_single_precision = tokens.astype(jnp.float32)
    inverse_root_mean = lax.rsqrt(
        jnp.mean(input_single_precision * input_single_precision, axis=-1, keepdims=True) + norm_eps
    )
    normalized_input = input_single_precision * inverse_root_mean
    rescaled_input = (normalized_input * gain_vector_row[None, :]).astype(jnp.bfloat16)

    flat_ids = routes.reshape(-1)
    one_hot = (flat_ids[:, None] == jnp.arange(experts, dtype=jnp.int32)[None, :]).astype(jnp.int32)
    slot_rank = jnp.sum((jnp.cumsum(one_hot, axis=0) - one_hot) * one_hot, axis=1)
    slot_index = (flat_ids * capacity + slot_rank).reshape(tok_count, top_count)
    slot_ids = jnp.arange(experts * capacity, dtype=jnp.int32)
    hits = slot_index[:, :, None] == slot_ids[None, None, :]
    placement = jnp.any(hits, axis=1)
    slot_weight = jnp.sum(jnp.where(hits, weights[:, :, None], 0.0), axis=(0, 1))
    placement_bf16 = placement.astype(jnp.bfloat16)
    pick = (((0,), (0,)), ((), ()))
    inputs_slab = lax.dot_general(
        rescaled_input, placement_bf16, pick, preferred_element_type=jnp.float32
    ).astype(jnp.bfloat16).T
    inputs_slab = row_major(inputs_slab)
    grads_slab = (
        lax.dot_general(incoming_gradient, placement_bf16, pick, preferred_element_type=jnp.float32)
        * slot_weight[None, :]
    ).astype(jnp.bfloat16).T
    grads_slab = row_major(grads_slab)
    arrived_inputs = exchange(inputs_slab, experts)
    arrived_grads = exchange(grads_slab, experts)
    computed = expert_backward(arrived_inputs, arrived_grads, gate_up, down_proj)
    returned = exchange(computed, experts)
    dnorm = jnp.dot(placement_bf16, returned, preferred_element_type=jnp.float32)
    normalized_input_gradient = dnorm * gain_vector_row[None, :]
    projected_rows = jnp.mean(normalized_input_gradient * normalized_input, axis=-1, keepdims=True)
    section_gradient = (
        incoming_gradient.astype(jnp.float32)
        + inverse_root_mean * (normalized_input_gradient - normalized_input * projected_rows)
    ).astype(jnp.bfloat16)
    return shifted(section_gradient[None], "section", -1)


def solution(mesh):
    return jax.shard_map(
        per_device,
        mesh=mesh,
        in_specs=(
            P("section", "expert", None),
            P("section", None),
            P("section", "expert", None),
            P("section", "expert", None),
            P("section", "expert", None),
            P("section", "expert", None, None),
            P("section", "expert", None, None),
        ),
        out_specs=P("section", "expert", None),
        check_vma=False,
    )
```

```python
import jax
import jax.numpy as jnp
from jax import lax
from jax.experimental.layout import Layout, with_layout_constraint
from jax.sharding import PartitionSpec as P

glu_alpha = 1.702
norm_eps = 1e-05
ROW_TILE = 8


def shifted(value, axis, steps):
    count = lax.axis_size(axis)
    pairs = [(source, (source + steps) % count) for source in range(count)]
    return lax.ppermute(value, axis, pairs)


def expert_backward(rows_in, grad_rows, gate_up, down_proj):
    preact = jnp.dot(rows_in, gate_up, preferred_element_type=jnp.float32)
    dact = lax.dot_general(
        grad_rows, down_proj, (((1,), (1,)), ((), ())), preferred_element_type=jnp.float32
    )
    half = down_proj.shape[0]
    gate = preact[:, :half]
    up_part = preact[:, half:]
    sig = jax.nn.sigmoid(glu_alpha * gate)
    dgate = dact * (up_part + 1.0) * (sig + glu_alpha * gate * sig * (1.0 - sig))
    dup = dact * gate * sig
    dpre = jnp.concatenate([dgate, dup], axis=1).astype(jnp.bfloat16)
    result_t = lax.dot_general(
        gate_up, dpre, (((1,), (1,)), ((), ())), preferred_element_type=jnp.float32
    )
    return row_major(result_t.astype(jnp.bfloat16).T)


def row_major(value):
    return with_layout_constraint(value, Layout(tuple(range(value.ndim))))


def exchange(slab):
    return lax.all_to_all(slab, "expert", split_axis=0, concat_axis=0, tiled=True)


def per_device(hidden_in, norm_gain, out_grad, expert_ids, route_weights, w_gate_up, w_down):
    tokens = hidden_in[0]
    gain_vector_row = norm_gain[0]
    incoming_gradient = out_grad[0]
    routes = expert_ids[0]
    weights = route_weights[0]
    gate_up = w_gate_up[0, 0]
    down_proj = w_down[0, 0]
    tok_count, feat_width = tokens.shape
    top_count = routes.shape[1]
    experts = lax.axis_size("expert")
    bound = max(2, tok_count * top_count * 5 // (4 * experts))
    capacity = -(-bound // ROW_TILE) * ROW_TILE

    input_single_precision = tokens.astype(jnp.float32)
    inverse_root_mean = lax.rsqrt(
        jnp.mean(input_single_precision * input_single_precision, axis=-1, keepdims=True) + norm_eps
    )
    normalized_input = input_single_precision * inverse_root_mean
    rescaled_input = (normalized_input * gain_vector_row[None, :]).astype(jnp.bfloat16)

    flat_ids = routes.reshape(-1)
    one_hot = (flat_ids[:, None] == jnp.arange(experts, dtype=jnp.int32)[None, :]).astype(jnp.int32)
    slot_rank = jnp.sum((jnp.cumsum(one_hot, axis=0) - one_hot) * one_hot, axis=1)
    slot_index = (flat_ids * capacity + slot_rank).reshape(tok_count, top_count)
    slot_ids = jnp.arange(experts * capacity, dtype=jnp.int32)
    hits = slot_index[:, :, None] == slot_ids[None, None, :]
    placement = jnp.any(hits, axis=1)
    slot_weight = jnp.sum(jnp.where(hits, weights[:, :, None], 0.0), axis=(0, 1))
    placement_bf16 = placement.astype(jnp.bfloat16)
    pick = (((0,), (0,)), ((), ()))
    inputs_slab = lax.dot_general(
        rescaled_input, placement_bf16, pick, preferred_element_type=jnp.float32
    ).astype(jnp.bfloat16).T
    inputs_slab = row_major(inputs_slab)
    grads_slab = (
        lax.dot_general(incoming_gradient, placement_bf16, pick, preferred_element_type=jnp.float32)
        * slot_weight[None, :]
    ).astype(jnp.bfloat16).T
    grads_slab = row_major(grads_slab)
    inputs_slab, grads_slab = lax.optimization_barrier((inputs_slab, grads_slab))
    arrived_inputs = exchange(inputs_slab.reshape(experts, capacity, feat_width))
    arrived_grads = exchange(grads_slab.reshape(experts, capacity, feat_width))
    computed = expert_backward(
        arrived_inputs.reshape(experts * capacity, feat_width),
        arrived_grads.reshape(experts * capacity, feat_width),
        gate_up,
        down_proj,
    )
    returned = exchange(computed.reshape(experts, capacity, feat_width)).reshape(
        experts * capacity, feat_width
    )
    dnorm = jnp.dot(placement_bf16, returned, preferred_element_type=jnp.float32)
    normalized_input_gradient = dnorm * gain_vector_row[None, :]
    projected_rows = jnp.mean(normalized_input_gradient * normalized_input, axis=-1, keepdims=True)
    section_gradient = (
        incoming_gradient.astype(jnp.float32)
        + inverse_root_mean * (normalized_input_gradient - normalized_input * projected_rows)
    ).astype(jnp.bfloat16)
    return shifted(section_gradient[None], "section", -1)


def solution(mesh):
    return jax.shard_map(
        per_device,
        mesh=mesh,
        in_specs=(
            P("section", "expert", None),
            P("section", None),
            P("section", "expert", None),
            P("section", "expert", None),
            P("section", "expert", None),
            P("section", "expert", None, None),
            P("section", "expert", None, None),
        ),
        out_specs=P("section", "expert", None),
        check_vma=False,
    )
```

```python
import jax
import jax.numpy as jnp
from jax.experimental import pallas as pl
from jax.experimental.pallas import tpu as pltpu
from jax import lax
from jax.experimental.layout import Layout, with_layout_constraint
from jax.sharding import PartitionSpec as P

glu_alpha = 1.702
norm_eps = 1e-05
ROW_TILE = 8
COL_TILE = 512


def shifted(value, axis, steps):
    count = lax.axis_size(axis)
    pairs = [(source, (source + steps) % count) for source in range(count)]
    return lax.ppermute(value, axis, pairs)


def expert_backward(rows_in, grad_rows, gate_up, down_proj):
    preact = jnp.dot(rows_in, gate_up, preferred_element_type=jnp.float32)
    dact = lax.dot_general(
        grad_rows, down_proj, (((1,), (1,)), ((), ())), preferred_element_type=jnp.float32
    )
    half = down_proj.shape[0]
    gate = preact[:, :half]
    up_part = preact[:, half:]
    sig = jax.nn.sigmoid(glu_alpha * gate)
    dgate = dact * (up_part + 1.0) * (sig + glu_alpha * gate * sig * (1.0 - sig))
    dup = dact * gate * sig
    dpre = jnp.concatenate([dgate, dup], axis=1).astype(jnp.bfloat16)
    return nt_matmul(dpre, gate_up)


def row_major(value):
    return with_layout_constraint(value, Layout(tuple(range(value.ndim))))


def nt_kernel(lhs_ref, rhs_ref, out_ref):
    out_ref[...] = lax.dot_general(
        lhs_ref[...], rhs_ref[...], (((1,), (1,)), ((), ())), preferred_element_type=jnp.float32
    ).astype(out_ref.dtype)


def nt_matmul(lhs, rhs):
    rows, depth = lhs.shape
    cols = rhs.shape[0]
    return pl.pallas_call(
        nt_kernel,
        grid=(pl.cdiv(cols, COL_TILE),),
        in_specs=[
            pl.BlockSpec((rows, depth), lambda j: (0, 0)),
            pl.BlockSpec((COL_TILE, depth), lambda j: (j, 0)),
        ],
        out_specs=pl.BlockSpec((rows, COL_TILE), lambda j: (0, j)),
        out_shape=jax.ShapeDtypeStruct((rows, cols), jnp.bfloat16),
        cost_estimate=pl.CostEstimate(
            flops=2 * rows * cols * depth,
            bytes_accessed=2 * (rows * depth + cols * depth + rows * cols),
            transcendentals=0,
        ),
    )(lhs, rhs)


def exchange(slab):
    return lax.all_to_all(slab, "expert", split_axis=0, concat_axis=0, tiled=True)


def per_device(hidden_in, norm_gain, out_grad, expert_ids, route_weights, w_gate_up, w_down):
    tokens = hidden_in[0]
    gain_vector_row = norm_gain[0]
    incoming_gradient = out_grad[0]
    routes = expert_ids[0]
    weights = route_weights[0]
    gate_up = w_gate_up[0, 0]
    down_proj = w_down[0, 0]
    tok_count, feat_width = tokens.shape
    top_count = routes.shape[1]
    experts = lax.axis_size("expert")
    bound = max(2, tok_count * top_count * 5 // (4 * experts))
    capacity = -(-bound // ROW_TILE) * ROW_TILE

    input_single_precision = tokens.astype(jnp.float32)
    inverse_root_mean = lax.rsqrt(
        jnp.mean(input_single_precision * input_single_precision, axis=-1, keepdims=True) + norm_eps
    )
    normalized_input = input_single_precision * inverse_root_mean
    rescaled_input = (normalized_input * gain_vector_row[None, :]).astype(jnp.bfloat16)

    flat_ids = routes.reshape(-1)
    one_hot = (flat_ids[:, None] == jnp.arange(experts, dtype=jnp.int32)[None, :]).astype(jnp.int32)
    slot_rank = jnp.sum((jnp.cumsum(one_hot, axis=0) - one_hot) * one_hot, axis=1)
    slot_index = (flat_ids * capacity + slot_rank).reshape(tok_count, top_count)
    slot_ids = jnp.arange(experts * capacity, dtype=jnp.int32)
    hits = slot_index[:, :, None] == slot_ids[None, None, :]
    placement = jnp.any(hits, axis=1)
    slot_weight = jnp.sum(jnp.where(hits, weights[:, :, None], 0.0), axis=(0, 1))
    placement_bf16 = placement.astype(jnp.bfloat16)
    pick = (((0,), (0,)), ((), ()))
    inputs_slab = lax.dot_general(
        rescaled_input, placement_bf16, pick, preferred_element_type=jnp.float32
    ).astype(jnp.bfloat16).T
    inputs_slab = row_major(inputs_slab)
    grads_slab = (
        lax.dot_general(incoming_gradient, placement_bf16, pick, preferred_element_type=jnp.float32)
        * slot_weight[None, :]
    ).astype(jnp.bfloat16).T
    grads_slab = row_major(grads_slab)
    inputs_slab, grads_slab = lax.optimization_barrier((inputs_slab, grads_slab))
    arrived_inputs = exchange(inputs_slab.reshape(experts, capacity, feat_width))
    arrived_grads = exchange(grads_slab.reshape(experts, capacity, feat_width))
    computed = expert_backward(
        arrived_inputs.reshape(experts * capacity, feat_width),
        arrived_grads.reshape(experts * capacity, feat_width),
        gate_up,
        down_proj,
    )
    returned = exchange(computed.reshape(experts, capacity, feat_width)).reshape(
        experts * capacity, feat_width
    )
    dnorm = jnp.dot(placement_bf16, returned, preferred_element_type=jnp.float32)
    normalized_input_gradient = dnorm * gain_vector_row[None, :]
    projected_rows = jnp.mean(normalized_input_gradient * normalized_input, axis=-1, keepdims=True)
    section_gradient = (
        incoming_gradient.astype(jnp.float32)
        + inverse_root_mean * (normalized_input_gradient - normalized_input * projected_rows)
    ).astype(jnp.bfloat16)
    return shifted(section_gradient[None], "section", -1)


def solution(mesh):
    return jax.shard_map(
        per_device,
        mesh=mesh,
        in_specs=(
            P("section", "expert", None),
            P("section", None),
            P("section", "expert", None),
            P("section", "expert", None),
            P("section", "expert", None),
            P("section", "expert", None, None),
            P("section", "expert", None, None),
        ),
        out_specs=P("section", "expert", None),
        check_vma=False,
    )
```

```python
import jax
import jax.numpy as jnp
from jax import lax
from jax.experimental.layout import Layout, with_layout_constraint
from jax.sharding import PartitionSpec as P

glu_alpha = 1.702
norm_eps = 1e-05
ROW_TILE = 8


def shifted(value, axis, steps):
    count = lax.axis_size(axis)
    pairs = [(source, (source + steps) % count) for source in range(count)]
    return lax.ppermute(value, axis, pairs)


def expert_backward(rows_in, grad_rows, gate_up, down_proj):
    preact = jnp.dot(rows_in, gate_up, preferred_element_type=jnp.float32)
    dact = lax.dot_general(
        grad_rows, down_proj, (((1,), (1,)), ((), ())), preferred_element_type=jnp.float32
    )
    half = down_proj.shape[0]
    gate = preact[:, :half]
    up_part = preact[:, half:]
    sig = jax.nn.sigmoid(glu_alpha * gate)
    dgate = dact * (up_part + 1.0) * (sig + glu_alpha * gate * sig * (1.0 - sig))
    dup = dact * gate * sig
    dpre = jnp.concatenate([dgate, dup], axis=1).astype(jnp.bfloat16)
    result_t = lax.dot_general(
        gate_up, dpre, (((1,), (1,)), ((), ())), preferred_element_type=jnp.float32
    )
    return row_major(result_t.astype(jnp.bfloat16).T)


def row_major(value):
    return with_layout_constraint(value, Layout(tuple(range(value.ndim))))


def exchange(slab):
    groups, slots, width = slab.shape
    quad = slab.reshape(groups, slots // 4, 4, width)
    moved = lax.all_to_all(quad, "expert", split_axis=0, concat_axis=0, tiled=True)
    return moved.reshape(groups, slots, width)


def per_device(hidden_in, norm_gain, out_grad, expert_ids, route_weights, w_gate_up, w_down):
    tokens = hidden_in[0]
    gain_vector_row = norm_gain[0]
    incoming_gradient = out_grad[0]
    routes = expert_ids[0]
    weights = route_weights[0]
    gate_up = w_gate_up[0, 0]
    down_proj = w_down[0, 0]
    tok_count, feat_width = tokens.shape
    top_count = routes.shape[1]
    experts = lax.axis_size("expert")
    bound = max(2, tok_count * top_count * 5 // (4 * experts))
    capacity = bound

    input_single_precision = tokens.astype(jnp.float32)
    inverse_root_mean = lax.rsqrt(
        jnp.mean(input_single_precision * input_single_precision, axis=-1, keepdims=True) + norm_eps
    )
    normalized_input = input_single_precision * inverse_root_mean
    rescaled_input = (normalized_input * gain_vector_row[None, :]).astype(jnp.bfloat16)

    flat_ids = routes.reshape(-1)
    one_hot = (flat_ids[:, None] == jnp.arange(experts, dtype=jnp.int32)[None, :]).astype(jnp.int32)
    slot_rank = jnp.sum((jnp.cumsum(one_hot, axis=0) - one_hot) * one_hot, axis=1)
    slot_index = (flat_ids * capacity + slot_rank).reshape(tok_count, top_count)
    slot_ids = jnp.arange(experts * capacity, dtype=jnp.int32)
    hits = slot_index[:, :, None] == slot_ids[None, None, :]
    placement = jnp.any(hits, axis=1)
    slot_weight = jnp.sum(jnp.where(hits, weights[:, :, None], 0.0), axis=(0, 1))
    placement_bf16 = placement.astype(jnp.bfloat16)
    pick = (((0,), (0,)), ((), ()))
    inputs_slab = lax.dot_general(
        rescaled_input, placement_bf16, pick, preferred_element_type=jnp.float32
    ).astype(jnp.bfloat16).T
    inputs_slab = row_major(inputs_slab)
    grads_slab = (
        lax.dot_general(incoming_gradient, placement_bf16, pick, preferred_element_type=jnp.float32)
        * slot_weight[None, :]
    ).astype(jnp.bfloat16).T
    grads_slab = row_major(grads_slab)
    inputs_slab, grads_slab = lax.optimization_barrier((inputs_slab, grads_slab))
    arrived_inputs = exchange(inputs_slab.reshape(experts, capacity, feat_width))
    arrived_grads = exchange(grads_slab.reshape(experts, capacity, feat_width))
    computed = expert_backward(
        arrived_inputs.reshape(experts * capacity, feat_width),
        arrived_grads.reshape(experts * capacity, feat_width),
        gate_up,
        down_proj,
    )
    returned = exchange(computed.reshape(experts, capacity, feat_width)).reshape(
        experts * capacity, feat_width
    )
    dnorm = jnp.dot(placement_bf16, returned, preferred_element_type=jnp.float32)
    normalized_input_gradient = dnorm * gain_vector_row[None, :]
    projected_rows = jnp.mean(normalized_input_gradient * normalized_input, axis=-1, keepdims=True)
    section_gradient = (
        incoming_gradient.astype(jnp.float32)
        + inverse_root_mean * (normalized_input_gradient - normalized_input * projected_rows)
    ).astype(jnp.bfloat16)
    return shifted(section_gradient[None], "section", -1)


def solution(mesh):
    return jax.shard_map(
        per_device,
        mesh=mesh,
        in_specs=(
            P("section", "expert", None),
            P("section", None),
            P("section", "expert", None),
            P("section", "expert", None),
            P("section", "expert", None),
            P("section", "expert", None, None),
            P("section", "expert", None, None),
        ),
        out_specs=P("section", "expert", None),
        check_vma=False,
    )
```

```python
import jax
import jax.numpy as jnp
from jax import lax
from jax.experimental.layout import Layout, with_layout_constraint
from jax.sharding import PartitionSpec as P

glu_alpha = 1.702
norm_eps = 1e-05
ROW_TILE = 8
QUAD = 4


def shifted(value, axis, steps):
    count = lax.axis_size(axis)
    pairs = [(source, (source + steps) % count) for source in range(count)]
    return lax.ppermute(value, axis, pairs)


def expert_backward(rows_in, grad_rows, gate_up, down_proj):
    last = rows_in.ndim - 1
    preact = lax.dot_general(
        rows_in, gate_up, (((last,), (0,)), ((), ())), preferred_element_type=jnp.float32
    )
    dact = lax.dot_general(
        grad_rows, down_proj, (((last,), (1,)), ((), ())), preferred_element_type=jnp.float32
    )
    half = down_proj.shape[0]
    gate = preact[..., :half]
    up_part = preact[..., half:]
    sig = jax.nn.sigmoid(glu_alpha * gate)
    dgate = dact * (up_part + 1.0) * (sig + glu_alpha * gate * sig * (1.0 - sig))
    dup = dact * gate * sig
    dpre = jnp.concatenate([dgate, dup], axis=last).astype(jnp.bfloat16)
    result = lax.dot_general(
        dpre, gate_up, (((last,), (1,)), ((), ())), preferred_element_type=jnp.float32
    )
    return row_major(result.astype(jnp.bfloat16))


def row_major(value):
    return with_layout_constraint(value, Layout(tuple(range(value.ndim))))


def exchange(slab, experts):
    groups, quad, width = slab.shape
    parted = slab.reshape(experts, groups // experts, quad, width)
    moved = lax.all_to_all(parted, "expert", split_axis=0, concat_axis=0, tiled=True)
    return moved.reshape(groups, quad, width)


def per_device(hidden_in, norm_gain, out_grad, expert_ids, route_weights, w_gate_up, w_down):
    tokens = hidden_in[0]
    gain_vector_row = norm_gain[0]
    incoming_gradient = out_grad[0]
    routes = expert_ids[0]
    weights = route_weights[0]
    gate_up = w_gate_up[0, 0]
    down_proj = w_down[0, 0]
    tok_count, feat_width = tokens.shape
    top_count = routes.shape[1]
    experts = lax.axis_size("expert")
    bound = max(2, tok_count * top_count * 5 // (4 * experts))
    capacity = bound

    input_single_precision = tokens.astype(jnp.float32)
    inverse_root_mean = lax.rsqrt(
        jnp.mean(input_single_precision * input_single_precision, axis=-1, keepdims=True) + norm_eps
    )
    normalized_input = input_single_precision * inverse_root_mean
    rescaled_input = (normalized_input * gain_vector_row[None, :]).astype(jnp.bfloat16)

    flat_ids = routes.reshape(-1)
    one_hot = (flat_ids[:, None] == jnp.arange(experts, dtype=jnp.int32)[None, :]).astype(jnp.int32)
    slot_rank = jnp.sum((jnp.cumsum(one_hot, axis=0) - one_hot) * one_hot, axis=1)
    slot_index = (flat_ids * capacity + slot_rank).reshape(tok_count, top_count)
    slot_ids = jnp.arange(experts * capacity, dtype=jnp.int32)
    hits = slot_index[:, :, None] == slot_ids[None, None, :]
    placement = jnp.any(hits, axis=1)
    slot_weight = jnp.sum(jnp.where(hits, weights[:, :, None], 0.0), axis=(0, 1))
    groups = experts * capacity // QUAD
    placement_quads = placement.astype(jnp.bfloat16).reshape(tok_count, groups, QUAD)
    pick = (((0,), (0,)), ((), ()))
    inputs_slab = row_major(
        lax.dot_general(placement_quads, rescaled_input, pick, preferred_element_type=jnp.float32)
        .astype(jnp.bfloat16)
    )
    grads_slab = row_major(
        (
            lax.dot_general(placement_quads, incoming_gradient, pick, preferred_element_type=jnp.float32)
            * slot_weight.reshape(groups, QUAD)[:, :, None]
        ).astype(jnp.bfloat16)
    )
    inputs_slab, grads_slab = lax.optimization_barrier((inputs_slab, grads_slab))
    arrived_inputs = exchange(inputs_slab, experts)
    arrived_grads = exchange(grads_slab, experts)
    computed = expert_backward(arrived_inputs, arrived_grads, gate_up, down_proj)
    returned = exchange(computed, experts)
    dnorm = lax.dot_general(
        placement_quads, returned, (((1, 2), (0, 1)), ((), ())), preferred_element_type=jnp.float32
    )
    normalized_input_gradient = dnorm * gain_vector_row[None, :]
    projected_rows = jnp.mean(normalized_input_gradient * normalized_input, axis=-1, keepdims=True)
    section_gradient = (
        incoming_gradient.astype(jnp.float32)
        + inverse_root_mean * (normalized_input_gradient - normalized_input * projected_rows)
    ).astype(jnp.bfloat16)
    return shifted(section_gradient[None], "section", -1)


def solution(mesh):
    return jax.shard_map(
        per_device,
        mesh=mesh,
        in_specs=(
            P("section", "expert", None),
            P("section", None),
            P("section", "expert", None),
            P("section", "expert", None),
            P("section", "expert", None),
            P("section", "expert", None, None),
            P("section", "expert", None, None),
        ),
        out_specs=P("section", "expert", None),
        check_vma=False,
    )
```

```python
import jax
import jax.numpy as jnp
from jax import lax
from jax.experimental.layout import Layout, with_layout_constraint
from jax.sharding import PartitionSpec as P

glu_alpha = 1.702
norm_eps = 1e-05
ROW_TILE = 8
QUAD = 4


def shifted(value, axis, steps):
    count = lax.axis_size(axis)
    pairs = [(source, (source + steps) % count) for source in range(count)]
    return lax.ppermute(value, axis, pairs)


def expert_backward(rows_in, grad_rows, gate_up, down_proj):
    last = rows_in.ndim - 1
    preact = lax.dot_general(
        rows_in, gate_up, (((last,), (0,)), ((), ())), preferred_element_type=jnp.float32
    )
    dact = lax.dot_general(
        grad_rows, down_proj, (((last,), (1,)), ((), ())), preferred_element_type=jnp.float32
    )
    half = down_proj.shape[0]
    gate = preact[..., :half]
    up_part = preact[..., half:]
    sig = jax.nn.sigmoid(glu_alpha * gate)
    dgate = dact * (up_part + 1.0) * (sig + glu_alpha * gate * sig * (1.0 - sig))
    dup = dact * gate * sig
    dpre = jnp.concatenate([dgate, dup], axis=last).astype(jnp.bfloat16)
    result = lax.dot_general(
        dpre, gate_up, (((last,), (1,)), ((), ())), preferred_element_type=jnp.float32
    )
    return row_major(result.astype(jnp.bfloat16))


def row_major(value):
    return with_layout_constraint(value, Layout(tuple(range(value.ndim))))


def exchange(slab, experts):
    groups, quad, width = slab.shape
    parted = slab.reshape(experts, groups // experts, quad, width)
    moved = lax.all_to_all(parted, "expert", split_axis=0, concat_axis=0, tiled=True)
    return moved.reshape(groups, quad, width)


def per_device(hidden_in, norm_gain, out_grad, expert_ids, route_weights, w_gate_up, w_down):
    tokens = hidden_in[0]
    gain_vector_row = norm_gain[0]
    incoming_gradient = out_grad[0]
    routes = expert_ids[0]
    weights = route_weights[0]
    gate_up = w_gate_up[0, 0]
    down_proj = w_down[0, 0]
    tok_count, feat_width = tokens.shape
    top_count = routes.shape[1]
    experts = lax.axis_size("expert")
    bound = max(2, tok_count * top_count * 5 // (4 * experts))
    capacity = bound

    input_single_precision = tokens.astype(jnp.float32)
    inverse_root_mean = lax.rsqrt(
        jnp.mean(input_single_precision * input_single_precision, axis=-1, keepdims=True) + norm_eps
    )
    normalized_input = input_single_precision * inverse_root_mean
    rescaled_input = (normalized_input * gain_vector_row[None, :]).astype(jnp.bfloat16)

    flat_ids = routes.reshape(-1)
    one_hot = (flat_ids[:, None] == jnp.arange(experts, dtype=jnp.int32)[None, :]).astype(jnp.int32)
    slot_rank = jnp.sum((jnp.cumsum(one_hot, axis=0) - one_hot) * one_hot, axis=1)
    slot_index = (flat_ids * capacity + slot_rank).reshape(tok_count, top_count)
    slot_ids = jnp.arange(experts * capacity, dtype=jnp.int32)
    hits = slot_index[:, :, None] == slot_ids[None, None, :]
    placement = jnp.any(hits, axis=1)
    slot_weight = jnp.sum(jnp.where(hits, weights[:, :, None], 0.0), axis=(0, 1))
    groups = experts * capacity // QUAD
    placement_quads = placement.astype(jnp.bfloat16).reshape(tok_count, groups, QUAD)
    pick = (((0,), (0,)), ((), ()))
    inputs_slab = row_major(
        lax.dot_general(placement_quads, rescaled_input, pick, preferred_element_type=jnp.float32)
        .astype(jnp.bfloat16)
    )
    scaled_rows = (weights[:, :, None] * incoming_gradient[:, None, :].astype(jnp.float32)).astype(
        jnp.bfloat16
    ).reshape(tok_count * top_count, feat_width)
    assignment_quads = (
        (slot_index.reshape(-1)[:, None] == slot_ids[None, :])
        .astype(jnp.bfloat16)
        .reshape(tok_count * top_count, groups, QUAD)
    )
    grads_slab = row_major(
        lax.dot_general(assignment_quads, scaled_rows, pick, preferred_element_type=jnp.float32)
        .astype(jnp.bfloat16)
    )
    inputs_slab, grads_slab = lax.optimization_barrier((inputs_slab, grads_slab))
    arrived_inputs = exchange(inputs_slab, experts)
    arrived_grads = exchange(grads_slab, experts)
    computed = expert_backward(arrived_inputs, arrived_grads, gate_up, down_proj)
    returned = exchange(computed, experts)
    dnorm = lax.dot_general(
        placement_quads, returned, (((1, 2), (0, 1)), ((), ())), preferred_element_type=jnp.float32
    )
    normalized_input_gradient = dnorm * gain_vector_row[None, :]
    projected_rows = jnp.mean(normalized_input_gradient * normalized_input, axis=-1, keepdims=True)
    section_gradient = (
        incoming_gradient.astype(jnp.float32)
        + inverse_root_mean * (normalized_input_gradient - normalized_input * projected_rows)
    ).astype(jnp.bfloat16)
    return shifted(section_gradient[None], "section", -1)


def solution(mesh):
    return jax.shard_map(
        per_device,
        mesh=mesh,
        in_specs=(
            P("section", "expert", None),
            P("section", None),
            P("section", "expert", None),
            P("section", "expert", None),
            P("section", "expert", None),
            P("section", "expert", None, None),
            P("section", "expert", None, None),
        ),
        out_specs=P("section", "expert", None),
        check_vma=False,
    )
```

```python
import jax
import jax.numpy as jnp
from jax import lax
from jax.experimental.layout import Layout, with_layout_constraint
from jax.sharding import PartitionSpec as P

glu_alpha = 1.702
norm_eps = 1e-05
ROW_TILE = 8
QUAD = 4


def shifted(value, axis, steps):
    count = lax.axis_size(axis)
    pairs = [(source, (source + steps) % count) for source in range(count)]
    return lax.ppermute(value, axis, pairs)


def expert_backward(rows_in, grad_rows, gate_up, down_proj):
    last = rows_in.ndim - 1
    preact = lax.dot_general(
        rows_in, gate_up, (((last,), (0,)), ((), ())), preferred_element_type=jnp.float32
    )
    dact = lax.dot_general(
        grad_rows, down_proj, (((last,), (1,)), ((), ())), preferred_element_type=jnp.float32
    )
    half = down_proj.shape[0]
    gate = preact[..., :half]
    up_part = preact[..., half:]
    sig = jax.nn.sigmoid(glu_alpha * gate)
    dgate = dact * (up_part + 1.0) * (sig + glu_alpha * gate * sig * (1.0 - sig))
    dup = dact * gate * sig
    dpre = jnp.concatenate([dgate, dup], axis=last).astype(jnp.bfloat16)
    result = lax.dot_general(
        dpre, gate_up, (((last,), (1,)), ((), ())), preferred_element_type=jnp.float32
    )
    return row_major(result.astype(jnp.bfloat16))


def row_major(value):
    return with_layout_constraint(value, Layout(tuple(range(value.ndim))))


def exchange(slab, experts):
    groups, quad, width = slab.shape
    parted = slab.reshape(experts, groups // experts, quad, width)
    moved = lax.all_to_all(parted, "expert", split_axis=0, concat_axis=0, tiled=True)
    return moved.reshape(groups, quad, width)


def per_device(hidden_in, norm_gain, out_grad, expert_ids, route_weights, w_gate_up, w_down):
    tokens = hidden_in[0]
    gain_vector_row = norm_gain[0]
    incoming_gradient = out_grad[0]
    routes = expert_ids[0]
    weights = route_weights[0]
    gate_up = w_gate_up[0, 0]
    down_proj = w_down[0, 0]
    tok_count, feat_width = tokens.shape
    top_count = routes.shape[1]
    experts = lax.axis_size("expert")
    bound = max(2, tok_count * top_count * 5 // (4 * experts))
    capacity = bound

    input_single_precision = tokens.astype(jnp.float32)
    inverse_root_mean = lax.rsqrt(
        jnp.mean(input_single_precision * input_single_precision, axis=-1, keepdims=True) + norm_eps
    )
    normalized_input = input_single_precision * inverse_root_mean
    rescaled_input = (normalized_input * gain_vector_row[None, :]).astype(jnp.bfloat16)

    flat_ids = routes.reshape(-1)
    one_hot = (flat_ids[:, None] == jnp.arange(experts, dtype=jnp.int32)[None, :]).astype(jnp.int32)
    slot_rank = jnp.sum((jnp.cumsum(one_hot, axis=0) - one_hot) * one_hot, axis=1)
    slot_index = (flat_ids * capacity + slot_rank).reshape(tok_count, top_count)
    slot_ids = jnp.arange(experts * capacity, dtype=jnp.int32)
    hits = slot_index[:, :, None] == slot_ids[None, None, :]
    placement = jnp.any(hits, axis=1)
    slot_weight = jnp.sum(jnp.where(hits, weights[:, :, None], 0.0), axis=(0, 1))
    groups = experts * capacity // QUAD
    placement_quads = placement.astype(jnp.bfloat16).reshape(tok_count, groups, QUAD)
    pick = (((0,), (0,)), ((), ()))
    inputs_slab = row_major(
        lax.dot_general(placement_quads, rescaled_input, pick, preferred_element_type=jnp.float32)
        .astype(jnp.bfloat16)
    )
    grads_slab = row_major(
        (
            lax.dot_general(placement_quads, incoming_gradient, pick, preferred_element_type=jnp.float32)
            * slot_weight.reshape(groups, QUAD)[:, :, None]
        ).astype(jnp.bfloat16)
    )
    arrived_inputs = exchange(inputs_slab, experts)
    arrived_grads = exchange(grads_slab, experts)
    computed = expert_backward(arrived_inputs, arrived_grads, gate_up, down_proj)
    returned = exchange(computed, experts)
    dnorm = lax.dot_general(
        placement_quads, returned, (((1, 2), (0, 1)), ((), ())), preferred_element_type=jnp.float32
    )
    normalized_input_gradient = dnorm * gain_vector_row[None, :]
    projected_rows = jnp.mean(normalized_input_gradient * normalized_input, axis=-1, keepdims=True)
    section_gradient = (
        incoming_gradient.astype(jnp.float32)
        + inverse_root_mean * (normalized_input_gradient - normalized_input * projected_rows)
    ).astype(jnp.bfloat16)
    return shifted(section_gradient[None], "section", -1)


def solution(mesh):
    return jax.shard_map(
        per_device,
        mesh=mesh,
        in_specs=(
            P("section", "expert", None),
            P("section", None),
            P("section", "expert", None),
            P("section", "expert", None),
            P("section", "expert", None),
            P("section", "expert", None, None),
            P("section", "expert", None, None),
        ),
        out_specs=P("section", "expert", None),
        check_vma=False,
    )
```

```python
import jax
import jax.numpy as jnp
from jax import lax
from jax.experimental.layout import Layout, with_layout_constraint
from jax.sharding import PartitionSpec as P

glu_alpha = 1.702
norm_eps = 1e-05
ROW_TILE = 8
QUAD = 4


def shifted(value, axis, steps):
    count = lax.axis_size(axis)
    pairs = [(source, (source + steps) % count) for source in range(count)]
    return lax.ppermute(value, axis, pairs)


def normalized_rows(raw_rows, gain_vector_row):
    rows = raw_rows.astype(jnp.float32)
    inverse_root_mean = lax.rsqrt(jnp.mean(rows * rows, axis=-1, keepdims=True) + norm_eps)
    return ((rows * inverse_root_mean) * gain_vector_row).astype(jnp.bfloat16)


def expert_backward(raw_rows, gain_vector_row, grad_rows, gate_up, down_proj):
    rows_in = normalized_rows(raw_rows, gain_vector_row)
    last = rows_in.ndim - 1
    preact = lax.dot_general(
        rows_in, gate_up, (((last,), (0,)), ((), ())), preferred_element_type=jnp.float32
    )
    dact = lax.dot_general(
        grad_rows, down_proj, (((last,), (1,)), ((), ())), preferred_element_type=jnp.float32
    )
    half = down_proj.shape[0]
    gate = preact[..., :half]
    up_part = preact[..., half:]
    sig = jax.nn.sigmoid(glu_alpha * gate)
    dgate = dact * (up_part + 1.0) * (sig + glu_alpha * gate * sig * (1.0 - sig))
    dup = dact * gate * sig
    dpre = jnp.concatenate([dgate, dup], axis=last).astype(jnp.bfloat16)
    result = lax.dot_general(
        dpre, gate_up, (((last,), (1,)), ((), ())), preferred_element_type=jnp.float32
    )
    return row_major(result.astype(jnp.bfloat16))


def row_major(value):
    return with_layout_constraint(value, Layout(tuple(range(value.ndim))))


def exchange(slab, experts):
    groups, quad, width = slab.shape
    parted = slab.reshape(experts, groups // experts, quad, width)
    moved = lax.all_to_all(parted, "expert", split_axis=0, concat_axis=0, tiled=True)
    return moved.reshape(groups, quad, width)


def per_device(hidden_in, norm_gain, out_grad, expert_ids, route_weights, w_gate_up, w_down):
    tokens = hidden_in[0]
    gain_vector_row = norm_gain[0]
    incoming_gradient = out_grad[0]
    routes = expert_ids[0]
    weights = route_weights[0]
    gate_up = w_gate_up[0, 0]
    down_proj = w_down[0, 0]
    tok_count, feat_width = tokens.shape
    top_count = routes.shape[1]
    experts = lax.axis_size("expert")
    bound = max(2, tok_count * top_count * 5 // (4 * experts))
    capacity = bound

    input_single_precision = tokens.astype(jnp.float32)
    inverse_root_mean = lax.rsqrt(
        jnp.mean(input_single_precision * input_single_precision, axis=-1, keepdims=True) + norm_eps
    )
    normalized_input = input_single_precision * inverse_root_mean

    flat_ids = routes.reshape(-1)
    one_hot = (flat_ids[:, None] == jnp.arange(experts, dtype=jnp.int32)[None, :]).astype(jnp.int32)
    slot_rank = jnp.sum((jnp.cumsum(one_hot, axis=0) - one_hot) * one_hot, axis=1)
    slot_index = (flat_ids * capacity + slot_rank).reshape(tok_count, top_count)
    slot_ids = jnp.arange(experts * capacity, dtype=jnp.int32)
    hits = slot_index[:, :, None] == slot_ids[None, None, :]
    placement = jnp.any(hits, axis=1)
    slot_weight = jnp.sum(jnp.where(hits, weights[:, :, None], 0.0), axis=(0, 1))
    groups = experts * capacity // QUAD
    placement_quads = placement.astype(jnp.bfloat16).reshape(tok_count, groups, QUAD)
    pick = (((0,), (0,)), ((), ()))
    inputs_slab = row_major(
        lax.dot_general(placement_quads, tokens, pick, preferred_element_type=jnp.float32)
        .astype(jnp.bfloat16)
    )
    grads_slab = row_major(
        (
            lax.dot_general(placement_quads, incoming_gradient, pick, preferred_element_type=jnp.float32)
            * slot_weight.reshape(groups, QUAD)[:, :, None]
        ).astype(jnp.bfloat16)
    )
    arrived_inputs = exchange(inputs_slab, experts)
    grads_slab, inverse_root_mean = lax.optimization_barrier((grads_slab, inverse_root_mean))
    arrived_grads = exchange(grads_slab, experts)
    computed = expert_backward(arrived_inputs, gain_vector_row, arrived_grads, gate_up, down_proj)
    returned = exchange(computed, experts)
    dnorm = lax.dot_general(
        placement_quads, returned, (((1, 2), (0, 1)), ((), ())), preferred_element_type=jnp.float32
    )
    normalized_input_gradient = dnorm * gain_vector_row[None, :]
    projected_rows = jnp.mean(normalized_input_gradient * normalized_input, axis=-1, keepdims=True)
    section_gradient = (
        incoming_gradient.astype(jnp.float32)
        + inverse_root_mean * (normalized_input_gradient - normalized_input * projected_rows)
    ).astype(jnp.bfloat16)
    return shifted(section_gradient[None], "section", -1)


def solution(mesh):
    return jax.shard_map(
        per_device,
        mesh=mesh,
        in_specs=(
            P("section", "expert", None),
            P("section", None),
            P("section", "expert", None),
            P("section", "expert", None),
            P("section", "expert", None),
            P("section", "expert", None, None),
            P("section", "expert", None, None),
        ),
        out_specs=P("section", "expert", None),
        check_vma=False,
    )
```

```python
import jax
import jax.numpy as jnp
from jax import lax
from jax.experimental.layout import Layout, with_layout_constraint
from jax.sharding import PartitionSpec as P

glu_alpha = 1.702
norm_eps = 1e-05
ROW_TILE = 8
QUAD = 4


def shifted(value, axis, steps):
    count = lax.axis_size(axis)
    pairs = [(source, (source + steps) % count) for source in range(count)]
    return lax.ppermute(value, axis, pairs)


def normalized_rows(raw_rows, gain_vector_row):
    rows = raw_rows.astype(jnp.float32)
    inverse_root_mean = lax.rsqrt(jnp.mean(rows * rows, axis=-1, keepdims=True) + norm_eps)
    return ((rows * inverse_root_mean) * gain_vector_row).astype(jnp.bfloat16)


def expert_backward(raw_rows, gain_vector_row, grad_rows, gate_up, down_proj):
    rows_in = normalized_rows(raw_rows, gain_vector_row)
    last = rows_in.ndim - 1
    preact = lax.dot_general(
        rows_in, gate_up, (((last,), (0,)), ((), ())), preferred_element_type=jnp.float32
    )
    dact = lax.dot_general(
        grad_rows, down_proj, (((last,), (1,)), ((), ())), preferred_element_type=jnp.float32
    )
    half = down_proj.shape[0]
    gate = preact[..., :half]
    up_part = preact[..., half:]
    sig = jax.nn.sigmoid(glu_alpha * gate)
    dgate = dact * (up_part + 1.0) * (sig + glu_alpha * gate * sig * (1.0 - sig))
    dup = dact * gate * sig
    dpre = jnp.concatenate([dgate, dup], axis=last).astype(jnp.bfloat16)
    result = lax.dot_general(
        dpre, gate_up, (((last,), (1,)), ((), ())), preferred_element_type=jnp.float32
    )
    return row_major(result.astype(jnp.bfloat16))


def row_major(value):
    return with_layout_constraint(value, Layout(tuple(range(value.ndim))))


def exchange(slab, experts):
    groups, quad, width = slab.shape
    parted = slab.reshape(experts, groups // experts, quad, width)
    moved = lax.all_to_all(parted, "expert", split_axis=0, concat_axis=0, tiled=True)
    return moved.reshape(groups, quad, width)


def per_device(hidden_in, norm_gain, out_grad, expert_ids, route_weights, w_gate_up, w_down):
    tokens = hidden_in[0]
    gain_vector_row = norm_gain[0]
    incoming_gradient = out_grad[0]
    routes = expert_ids[0]
    weights = route_weights[0]
    gate_up = w_gate_up[0, 0]
    down_proj = w_down[0, 0]
    tok_count, feat_width = tokens.shape
    top_count = routes.shape[1]
    experts = lax.axis_size("expert")
    bound = max(2, tok_count * top_count * 5 // (4 * experts))
    capacity = bound

    input_single_precision = tokens.astype(jnp.float32)
    inverse_root_mean = lax.rsqrt(
        jnp.mean(input_single_precision * input_single_precision, axis=-1, keepdims=True) + norm_eps
    )
    normalized_input = input_single_precision * inverse_root_mean

    flat_ids = routes.reshape(-1)
    one_hot = (flat_ids[:, None] == jnp.arange(experts, dtype=jnp.int32)[None, :]).astype(jnp.bfloat16)
    order = jnp.arange(flat_ids.shape[0], dtype=jnp.int32)
    earlier = (order[:, None] > order[None, :]).astype(jnp.bfloat16)
    prior = jnp.dot(earlier, one_hot, preferred_element_type=jnp.float32)
    slot_rank = jnp.sum(prior * one_hot.astype(jnp.float32), axis=1).astype(jnp.int32)
    slot_index = (flat_ids * capacity + slot_rank).reshape(tok_count, top_count)
    slot_ids = jnp.arange(experts * capacity, dtype=jnp.int32)
    hits = slot_index[:, :, None] == slot_ids[None, None, :]
    placement = jnp.any(hits, axis=1)
    slot_weight = jnp.sum(jnp.where(hits, weights[:, :, None], 0.0), axis=(0, 1))
    groups = experts * capacity // QUAD
    placement_quads = placement.astype(jnp.bfloat16).reshape(tok_count, groups, QUAD)
    pick = (((0,), (0,)), ((), ()))
    inputs_slab = row_major(
        lax.dot_general(placement_quads, tokens, pick, preferred_element_type=jnp.float32)
        .astype(jnp.bfloat16)
    )
    grads_slab = row_major(
        (
            lax.dot_general(placement_quads, incoming_gradient, pick, preferred_element_type=jnp.float32)
            * slot_weight.reshape(groups, QUAD)[:, :, None]
        ).astype(jnp.bfloat16)
    )
    arrived_inputs = exchange(inputs_slab, experts)
    grads_slab, inverse_root_mean = lax.optimization_barrier((grads_slab, inverse_root_mean))
    arrived_grads = exchange(grads_slab, experts)
    computed = expert_backward(arrived_inputs, gain_vector_row, arrived_grads, gate_up, down_proj)
    returned = exchange(computed, experts)
    dnorm = lax.dot_general(
        placement_quads, returned, (((1, 2), (0, 1)), ((), ())), preferred_element_type=jnp.float32
    )
    normalized_input_gradient = dnorm * gain_vector_row[None, :]
    projected_rows = jnp.mean(normalized_input_gradient * normalized_input, axis=-1, keepdims=True)
    section_gradient = (
        incoming_gradient.astype(jnp.float32)
        + inverse_root_mean * (normalized_input_gradient - normalized_input * projected_rows)
    ).astype(jnp.bfloat16)
    return shifted(section_gradient[None], "section", -1)


def solution(mesh):
    return jax.shard_map(
        per_device,
        mesh=mesh,
        in_specs=(
            P("section", "expert", None),
            P("section", None),
            P("section", "expert", None),
            P("section", "expert", None),
            P("section", "expert", None),
            P("section", "expert", None, None),
            P("section", "expert", None, None),
        ),
        out_specs=P("section", "expert", None),
        check_vma=False,
    )
```

```python
import jax
import jax.numpy as jnp
from jax import lax
from jax.experimental.layout import Layout, with_layout_constraint
from jax.sharding import PartitionSpec as P

glu_alpha = 1.702
norm_eps = 1e-05
ROW_TILE = 8
QUAD = 4


def shifted(value, axis, steps):
    count = lax.axis_size(axis)
    pairs = [(source, (source + steps) % count) for source in range(count)]
    return lax.ppermute(value, axis, pairs)


def normalized_rows(raw_rows, gain_vector_row):
    rows = raw_rows.astype(jnp.float32)
    inverse_root_mean = lax.rsqrt(jnp.mean(rows * rows, axis=-1, keepdims=True) + norm_eps)
    return ((rows * inverse_root_mean) * gain_vector_row).astype(jnp.bfloat16)


def expert_backward(raw_rows, gain_vector_row, grad_rows, gate_up, down_proj):
    rows_in = normalized_rows(raw_rows, gain_vector_row)
    last = rows_in.ndim - 1
    preact = lax.dot_general(
        rows_in, gate_up, (((last,), (0,)), ((), ())), preferred_element_type=jnp.float32
    )
    dact = lax.dot_general(
        grad_rows, down_proj, (((last,), (1,)), ((), ())), preferred_element_type=jnp.float32
    )
    half = down_proj.shape[0]
    gate = preact[..., :half]
    up_part = preact[..., half:]
    sig = jax.nn.sigmoid(glu_alpha * gate)
    dgate = dact * (up_part + 1.0) * (sig + glu_alpha * gate * sig * (1.0 - sig))
    dup = dact * gate * sig
    dpre = jnp.concatenate([dgate, dup], axis=last).astype(jnp.bfloat16)
    result = lax.dot_general(
        dpre, gate_up, (((last,), (1,)), ((), ())), preferred_element_type=jnp.float32
    )
    return row_major(result.astype(jnp.bfloat16))


def row_major(value):
    return with_layout_constraint(value, Layout(tuple(range(value.ndim))))


def exchange(slab, experts):
    groups, quad, width = slab.shape
    parted = slab.reshape(experts, groups // experts, quad, width)
    moved = lax.all_to_all(parted, "expert", split_axis=0, concat_axis=0, tiled=True)
    return moved.reshape(groups, quad, width)


def per_device(hidden_in, norm_gain, out_grad, expert_ids, route_weights, w_gate_up, w_down):
    tokens = hidden_in[0]
    gain_vector_row = norm_gain[0]
    incoming_gradient = out_grad[0]
    routes = expert_ids[0]
    weights = route_weights[0]
    gate_up = w_gate_up[0, 0]
    down_proj = w_down[0, 0]
    tok_count, feat_width = tokens.shape
    top_count = routes.shape[1]
    experts = lax.axis_size("expert")
    bound = max(2, tok_count * top_count * 5 // (4 * experts))
    capacity = bound

    input_single_precision = tokens.astype(jnp.float32)
    inverse_root_mean = lax.rsqrt(
        jnp.mean(input_single_precision * input_single_precision, axis=-1, keepdims=True) + norm_eps
    )
    normalized_input = input_single_precision * inverse_root_mean

    flat_ids = routes.T.reshape(-1)
    one_hot = (flat_ids[:, None] == jnp.arange(experts, dtype=jnp.int32)[None, :]).astype(jnp.bfloat16)
    order = jnp.arange(flat_ids.shape[0], dtype=jnp.int32)
    earlier = (order[:, None] > order[None, :]).astype(jnp.bfloat16)
    prior = jnp.dot(earlier, one_hot, preferred_element_type=jnp.float32)
    slot_rank = jnp.sum(prior * one_hot.astype(jnp.float32), axis=1).astype(jnp.int32)
    slot_index = (flat_ids * capacity + slot_rank).reshape(top_count, tok_count).T
    slot_ids = jnp.arange(experts * capacity, dtype=jnp.int32)
    hits = slot_index[:, :, None] == slot_ids[None, None, :]
    placement = jnp.any(hits, axis=1)
    slot_weight = jnp.sum(jnp.where(hits, weights[:, :, None], 0.0), axis=(0, 1))
    groups = experts * capacity // QUAD
    placement_quads = placement.astype(jnp.bfloat16).reshape(tok_count, groups, QUAD)
    pick = (((0,), (0,)), ((), ()))
    inputs_slab = row_major(
        lax.dot_general(placement_quads, tokens, pick, preferred_element_type=jnp.float32)
        .astype(jnp.bfloat16)
    )
    grads_slab = row_major(
        (
            lax.dot_general(placement_quads, incoming_gradient, pick, preferred_element_type=jnp.float32)
            * slot_weight.reshape(groups, QUAD)[:, :, None]
        ).astype(jnp.bfloat16)
    )
    arrived_inputs = exchange(inputs_slab, experts)
    grads_slab, inverse_root_mean = lax.optimization_barrier((grads_slab, inverse_root_mean))
    arrived_grads = exchange(grads_slab, experts)
    computed = expert_backward(arrived_inputs, gain_vector_row, arrived_grads, gate_up, down_proj)
    returned = exchange(computed, experts)
    dnorm = lax.dot_general(
        placement_quads, returned, (((1, 2), (0, 1)), ((), ())), preferred_element_type=jnp.float32
    )
    normalized_input_gradient = dnorm * gain_vector_row[None, :]
    projected_rows = jnp.mean(normalized_input_gradient * normalized_input, axis=-1, keepdims=True)
    section_gradient = (
        incoming_gradient.astype(jnp.float32)
        + inverse_root_mean * (normalized_input_gradient - normalized_input * projected_rows)
    ).astype(jnp.bfloat16)
    return shifted(section_gradient[None], "section", -1)


def solution(mesh):
    return jax.shard_map(
        per_device,
        mesh=mesh,
        in_specs=(
            P("section", "expert", None),
            P("section", None),
            P("section", "expert", None),
            P("section", "expert", None),
            P("section", "expert", None),
            P("section", "expert", None, None),
            P("section", "expert", None, None),
        ),
        out_specs=P("section", "expert", None),
        check_vma=False,
    )
```
